256 devices in a mesh: person: 2 (over x_lo), tm: 32 (over y, z), mp: 4 (over x_hi, core).
Axes of the slice: x: 4 (x_hi: 2, x_lo: 2; x = x_hi * 2 + x_lo), y: 4, z: 8, core: 2. Of those that a mesh axis runs over, the one named last changes fastest.
Arguments:
- motion: bfloat16 [2, 2, 8192, 2048], P('person', None, 'tm', 'mp'), may hold values from -6 to 6
- valid: int32 [2, 2, 8192], P('person', None, 'tm'), may hold values from 0 to 1, as said below
- windows: int32 [32], replicated, may hold values from 64 to 512, as said below
- gains: float32 [2, 2048], replicated, may hold values from 0.5 to 1.5
- w_self_in: bfloat16 [2048, 3072], P('tm', 'mp')
- w_self_out: bfloat16 [2048, 2048], P('mp', 'tm'), may hold values from -0.125 to 0.125
- w_cross_in: bfloat16 [2048, 3072], P('tm', 'mp')
- w_cross_out: bfloat16 [2048, 2048], P('mp', 'tm'), may hold values from -0.125 to 0.125
Outputs:
- mixed: bfloat16 [2, 2, 8192, 2048], P('person', None, 'tm', 'mp')
The draws below stay inside these ranges and needn't reach their ends.
Inputs may be any that keep to these rules, and one draw needn't show every extreme that they name: `valid`: for each person and clip the frames with 1 form a prefix that covers at least half of the 8192 frames and never all of them. `windows`: some head's window is exactly 512.
All inputs are finite; a program needn't handle non-finite values.
Results may differ from the reference program's by a relative error of at most 0.035.
The reference program's roundings to bfloat16 on the way count: a program that leaves them out, or rounds other values in their place, can miss the bound.
Values may be sent and summed in bfloat16 or wider, within the bound.
No kernel may reach another device: no remote copies, remote signals or barrier semaphores. Data moves between devices by JAX's collectives and lax.ppermute only.
A program may use at most 64 MiB of HBM per device.

```python
import jax
import jax.numpy as jnp
from jax import lax

D = 2048
HEADS = 32
KV_HEADS = 8
HEAD_DIM = 64
WIN = 512
FRAMES_DEV = 256
CLIPS = 2
PERSONS = 2
FRAMES = 8192


def in_weight(key):
    group = HEADS // KV_HEADS
    base = jax.random.normal(key, (D, KV_HEADS, group + 2, HEAD_DIM), jnp.float32) * D ** (-0.5)
    return base.reshape(D, KV_HEADS * (group + 2) * HEAD_DIM).astype(jnp.bfloat16)


def draw_w_self_in(key, part):
    return in_weight(jax.random.fold_in(key, 11))


def draw_w_cross_in(key, part):
    return in_weight(jax.random.fold_in(key, 23))


def draw_valid(key, part):
    half = FRAMES // 2
    lengths = half + jax.random.randint(jax.random.fold_in(key, 5), (PERSONS, CLIPS), 0, FRAMES - half)
    frame_index = jnp.arange(FRAMES, dtype=jnp.int32)
    return (frame_index[None, None, :] < lengths[:, :, None]).astype(jnp.int32)


def draw_windows(key, part):
    spans = jax.random.randint(jax.random.fold_in(key, 7), (HEADS,), WIN // 8, WIN + 1)
    chosen = jax.random.randint(jax.random.fold_in(key, 9), (), 0, HEADS)
    return jnp.where(jnp.arange(HEADS, dtype=jnp.int32) == chosen, WIN, spans).astype(jnp.int32)


def level_of(key, extent, pieces, low, high):
    level, own = 1.0, jax.random.fold_in(key, 6)
    for axis_at, blocks in pieces:
        heights = jnp.exp(jax.random.uniform(jax.random.fold_in(own, axis_at), (blocks,), jnp.float32, low / len(pieces), high / len(pieces)))
        level = level * jnp.repeat(heights, extent[axis_at] // blocks).reshape([-1 if axis == axis_at else 1 for axis in range(len(extent))])
    return level


def bell_draw(rng, shape, spread, most, split=(), kind=jnp.bfloat16):
    array = jax.random.normal(rng, shape, jnp.float32) * spread
    if len(split) > 0:
        array = level_of(rng, shape, split, -0.22, 0.18) * array
    return jnp.clip(array, min=-most, max=most).astype(kind)


def setup_inputs(seed: int = 0) -> dict:
    seeds = jax.random.split(jax.random.key(seed), 9)
    return {
        "motion": bell_draw(seeds[0], (PERSONS, CLIPS, FRAMES, D), 1.0, 6.0, ((0, 2), (2, 32), (3, 4))),
        "valid": draw_valid(jax.random.fold_in(seeds[8], 71), 0),
        "windows": draw_windows(jax.random.fold_in(seeds[8], 71), 0),
        "gains": jnp.clip(1.0 + 0.1 * jax.random.normal(seeds[3], (2, D), jnp.float32), 0.5, 1.5),
        "w_self_in": draw_w_self_in(jax.random.fold_in(seeds[8], 71), 0),
        "w_self_out": bell_draw(seeds[5], (HEADS * HEAD_DIM, D), (HEADS * HEAD_DIM) ** -0.5, 0.125, ((0, 4), (1, 32))),
        "w_cross_in": draw_w_cross_in(jax.random.fold_in(seeds[8], 71), 0),
        "w_cross_out": bell_draw(seeds[7], (HEADS * HEAD_DIM, D), (HEADS * HEAD_DIM) ** -0.5, 0.125, ((0, 4), (1, 32))),
    }


EPS = 1e-05

def rms_normed(rows, gain):
    values = rows.astype(jnp.float32)
    scale = lax.rsqrt(lax.optimization_barrier(jnp.mean(values * values, axis=-1, keepdims=True)) + EPS)
    return (values * scale * gain).astype(jnp.bfloat16)

def attend_block(queries, keys, values, key_valid, wins):
    count_q = queries.shape[0]
    count_k = keys.shape[0]
    dist = jnp.arange(count_q)[:, None] + (count_k - count_q) - jnp.arange(count_k)[None, :]
    allowed = (dist >= 0) & (dist < wins[:, :, None, None]) & ((key_valid[None, None, None, :] == 1) | (dist == 0))
    scores = jnp.einsum('qkgd,ckd->kgqc', queries.astype(jnp.float32), keys.astype(jnp.float32)) * HEAD_DIM ** (-0.5)
    top = lax.optimization_barrier(jnp.max(jnp.where(allowed, scores, -1e+30), axis=-1, keepdims=True))
    exps = jnp.where(allowed, jnp.exp(scores - top), 0.0)
    total = lax.optimization_barrier(jnp.sum(exps, axis=-1))
    weights = exps.astype(jnp.bfloat16)
    summed = jnp.einsum('kgqc,ckd->qkgd', weights.astype(jnp.float32), values.astype(jnp.float32))
    return (summed / jnp.transpose(total, (2, 0, 1))[..., None]).astype(jnp.bfloat16)

def attend_all(qproj, kproj, key_valid, windows):
    group = HEADS // KV_HEADS
    wins = windows.reshape(KV_HEADS, group)
    streams = qproj.shape[0] * qproj.shape[1]

    def attend_stream(items):
        qrows, krows, kvalid = items
        qshape = qrows.reshape(FRAMES, KV_HEADS, group + 2, HEAD_DIM)
        kshape = krows.reshape(FRAMES, KV_HEADS, group + 2, HEAD_DIM)
        queries = qshape[:, :, :group]
        zeros_kv = jnp.zeros((WIN, KV_HEADS, HEAD_DIM), krows.dtype)
        keys = jnp.concatenate([zeros_kv, kshape[:, :, group]], 0)
        values = jnp.concatenate([zeros_kv, kshape[:, :, group + 1]], 0)
        masks = jnp.concatenate([jnp.zeros((WIN,), jnp.int32), kvalid.astype(jnp.int32)], 0)

        def one_block(index):
            start = (index * FRAMES_DEV).astype(jnp.int32)
            qblock = lax.dynamic_slice_in_dim(queries, start, FRAMES_DEV, 0)
            kblock = lax.dynamic_slice_in_dim(keys, start, FRAMES_DEV + WIN, 0)
            vblock = lax.dynamic_slice_in_dim(values, start, FRAMES_DEV + WIN, 0)
            mblock = lax.dynamic_slice_in_dim(masks, start, FRAMES_DEV + WIN, 0)
            return attend_block(qblock, kblock, vblock, mblock, wins)
        blocks = lax.map(one_block, jnp.arange(FRAMES // FRAMES_DEV, dtype=jnp.int32))
        return blocks.reshape(FRAMES, HEADS * HEAD_DIM)
    outputs = lax.map(attend_stream, (qproj.reshape(streams, FRAMES, -1), kproj.reshape(streams, FRAMES, -1), key_valid.reshape(streams, FRAMES)))
    return outputs.reshape(qproj.shape[0], qproj.shape[1], FRAMES, HEADS * HEAD_DIM)

def reference(motion, valid, windows, gains, w_self_in, w_self_out, w_cross_in, w_cross_out):
    shape = motion.shape
    normed = rms_normed(motion, gains[0])
    self_proj = jnp.dot(normed.reshape(-1, D), w_self_in, preferred_element_type=jnp.float32).astype(jnp.bfloat16)
    self_proj = self_proj.reshape(shape[0], shape[1], shape[2], -1)
    self_heads = attend_all(self_proj, self_proj, valid, windows)
    self_out = jnp.dot(self_heads.reshape(-1, HEADS * HEAD_DIM), w_self_out, preferred_element_type=jnp.float32)
    hidden = (motion.astype(jnp.float32) + self_out.reshape(shape)).astype(jnp.bfloat16)
    normed2 = rms_normed(hidden, gains[1])
    cross_proj = jnp.dot(normed2.reshape(-1, D), w_cross_in, preferred_element_type=jnp.float32).astype(jnp.bfloat16)
    cross_proj = cross_proj.reshape(shape[0], shape[1], shape[2], -1)
    cross_heads = attend_all(cross_proj, cross_proj[::-1], valid[::-1], windows)
    cross_out = jnp.dot(cross_heads.reshape(-1, HEADS * HEAD_DIM), w_cross_out, preferred_element_type=jnp.float32)
    return (hidden.astype(jnp.float32) + cross_out.reshape(shape)).astype(jnp.bfloat16)
```

```python
import jax
import jax.numpy as jnp
from jax import lax
from jax.sharding import PartitionSpec as P

D = 2048
HEADS = 32
KV_HEADS = 8
HEAD_DIM = 64
WIN = 512


EPS = 1e-05


def passed_along(value, axis, steps):
    count = lax.axis_size(axis)
    leading, last = (max(0, -steps), min(count, count - steps))
    return lax.ppermute(value, axis, [(source, source + steps) for source in range(leading, last)])


def swapped(value, axis, mask):
    pairs = [(source, source ^ mask) for source in range(lax.axis_size(axis))]
    return lax.ppermute(value, axis, pairs)


def gathered_mp(block):
    count = lax.axis_size("mp")
    me = lax.axis_index("mp")
    width = block.shape[-1]
    full = jnp.zeros(block.shape[:-1] + (width * count,), block.dtype)
    zeros = (0,) * (block.ndim - 1)
    full = lax.dynamic_update_slice(full, block, zeros + (me * width,))
    for mask in range(1, count):
        piece = swapped(block, "mp", mask)
        full = lax.dynamic_update_slice(full, piece, zeros + ((me ^ mask) * width,))
    return full


def rms_normed(rows, gain):
    values = rows.astype(jnp.float32)
    scale = lax.rsqrt(jnp.mean(values * values, axis=-1, keepdims=True) + EPS)
    return (values * scale * gain).astype(jnp.bfloat16)


def project_in(normed_rows, weight_rows):
    total = jnp.dot(
        normed_rows,
        lax.all_gather(weight_rows, "tm", axis=0, tiled=True),
        preferred_element_type=jnp.float32,
    )
    return total.astype(jnp.bfloat16)


def out_weight(weight):
    count = lax.axis_size("mp")
    me = lax.axis_index("mp")
    rows = lax.all_gather(weight, "tm", axis=1, tiled=True)
    width = rows.shape[1] // count
    pieces = [lax.dynamic_slice_in_dim(rows, me * width, width, 1)]
    for mask in range(1, count):
        part = lax.dynamic_slice_in_dim(rows, (me ^ mask) * width, width, 1)
        pieces.append(swapped(part, "mp", mask))
    return jnp.concatenate(pieces, 0)


def project_out(heads, weight_pieces, residual):
    count = lax.axis_size("mp")
    pieces = [heads] + [swapped(heads, "mp", mask) for mask in range(1, count)]
    terms = jnp.dot(
        jnp.concatenate(pieces, 1), weight_pieces, preferred_element_type=jnp.float32
    )
    return (residual.astype(jnp.float32) + terms).astype(jnp.bfloat16)


def earlier_frames(pair, frames):
    pieces = [pair]
    for step in range(1, WIN // frames + 1):
        pieces.insert(0, passed_along((pair[0], pair[1]), "tm", step))
    key_vals = jnp.concatenate([piece[0] for piece in pieces], 1)
    masks = jnp.concatenate([piece[1] for piece in pieces], 1)
    return (key_vals, masks)


def window_attend(queries, key_vals, masks, wins):
    count_q = queries.shape[1]
    count_k = key_vals.shape[1]
    dist = jnp.arange(count_q)[:, None] + (count_k - count_q) - jnp.arange(count_k)[None, :]

    def one_clip(items):
        query, pairs, kvalid = items
        keys = pairs[:, :, 0]
        values = pairs[:, :, 1]
        allowed = (
            (dist >= 0)
            & (dist < wins[:, :, None, None])
            & ((kvalid[None, None, None, :] == 1) | (dist == 0))
        )
        scores = jnp.einsum(
            "qkgd,ckd->kgqc", query, keys, preferred_element_type=jnp.float32
        ) * HEAD_DIM ** (-0.5)
        top = jnp.max(jnp.where(allowed, scores, -1e30), axis=-1, keepdims=True)
        exps = jnp.where(allowed, jnp.exp(scores - top), 0.0)
        total = jnp.sum(exps, axis=-1)
        weights = exps.astype(jnp.bfloat16)
        summed = jnp.einsum("kgqc,ckd->qkgd", weights, values, preferred_element_type=jnp.float32)
        return (summed / jnp.transpose(total, (2, 0, 1))[..., None]).astype(jnp.bfloat16)

    outputs = lax.map(one_clip, (queries, key_vals, masks))
    return outputs.reshape(outputs.shape[0] * outputs.shape[1], -1)


def body(motion, valid, windows, gains, w_self_in, w_self_out, w_cross_in, w_cross_out):
    clips = motion.shape[1]
    frames = motion.shape[2]
    count = clips * frames
    group = HEADS // KV_HEADS
    local_heads = w_self_out.shape[0] // HEAD_DIM
    local_groups = local_heads // group
    wins = lax.dynamic_slice_in_dim(
        windows, lax.axis_index("mp") * local_heads, local_heads, 0
    ).reshape(local_groups, group)
    own_valid = valid[0]
    residual = motion.reshape(count, motion.shape[3])
    self_out_w = out_weight(w_self_out)
    cross_out_w = out_weight(w_cross_out)
    full = gathered_mp(residual)
    normed = rms_normed(full, gains[0])
    self_proj = project_in(normed, w_self_in).reshape(
        clips, frames, local_groups, group + 2, HEAD_DIM
    )
    self_pair = self_proj[:, :, :, group:]
    key_vals, masks = earlier_frames((self_pair, own_valid), frames)
    self_heads = window_attend(self_proj[:, :, :, :group], key_vals, masks, wins)
    hidden = project_out(self_heads, self_out_w, residual)
    hidden_full = gathered_mp(hidden)
    normed2 = rms_normed(hidden_full, gains[1])
    cross_proj = project_in(normed2, w_cross_in).reshape(
        clips, frames, local_groups, group + 2, HEAD_DIM
    )
    cross_pair = cross_proj[:, :, :, group:]
    partner = swapped((cross_pair, own_valid), "person", 1)
    partner_vals, partner_masks = earlier_frames(partner, frames)
    cross_heads = window_attend(cross_proj[:, :, :, :group], partner_vals, partner_masks, wins)
    mixed = project_out(cross_heads, cross_out_w, hidden)
    return mixed.reshape(motion.shape)


def solution(mesh):
    in_specs = (
        P("person", None, "tm", "mp"),
        P("person", None, "tm"),
        P(),
        P(),
        P("tm", "mp"),
        P("mp", "tm"),
        P("tm", "mp"),
        P("mp", "tm"),
    )
    out_specs = P("person", None, "tm", "mp")
    return jax.shard_map(body, mesh=mesh, in_specs=in_specs, out_specs=out_specs, check_vma=False)
```

```python
import jax
import jax.numpy as jnp
from jax import lax
from jax.sharding import PartitionSpec as P

D = 2048
HEADS = 32
KV_HEADS = 8
HEAD_DIM = 64
WIN = 512


EPS = 1e-05


def passed_along(value, axis, steps):
    count = lax.axis_size(axis)
    leading, last = (max(0, -steps), min(count, count - steps))
    return lax.ppermute(value, axis, [(source, source + steps) for source in range(leading, last)])


def swapped(value, axis, mask):
    pairs = [(source, source ^ mask) for source in range(lax.axis_size(axis))]
    return lax.ppermute(value, axis, pairs)


def gathered_mp(block):
    count = lax.axis_size("mp")
    me = lax.axis_index("mp")
    width = block.shape[-1]
    full = jnp.zeros(block.shape[:-1] + (width * count,), block.dtype)
    zeros = (0,) * (block.ndim - 1)
    full = lax.dynamic_update_slice(full, block, zeros + (me * width,))
    for mask in range(1, count):
        piece = swapped(block, "mp", mask)
        full = lax.dynamic_update_slice(full, piece, zeros + ((me ^ mask) * width,))
    return full


def rms_normed(rows, gain):
    values = rows.astype(jnp.float32)
    scale = lax.rsqrt(jnp.mean(values * values, axis=-1, keepdims=True) + EPS)
    return (values * scale * gain).astype(jnp.bfloat16)


def split_gather(weight, axis, gather_axis):
    me = lax.axis_index("person")
    half = weight.shape[axis] // 2
    own = lax.all_gather(
        lax.dynamic_slice_in_dim(weight, me * half, half, axis), "tm", axis=gather_axis, tiled=True
    )
    other = swapped(own, "person", 1)
    shape = list(own.shape)
    shape[axis] *= 2
    full = jnp.zeros(shape, own.dtype)
    full = lax.dynamic_update_slice_in_dim(full, own, me * half, axis)
    return lax.dynamic_update_slice_in_dim(full, other, (1 - me) * half, axis)


def project_in(normed_rows, weight_rows):
    total = jnp.dot(
        normed_rows,
        split_gather(weight_rows, 1, 0),
        preferred_element_type=jnp.float32,
    )
    return total.astype(jnp.bfloat16)


def out_weight(weight):
    count = lax.axis_size("mp")
    me = lax.axis_index("mp")
    rows = split_gather(weight, 0, 1)
    width = rows.shape[1] // count
    pieces = [lax.dynamic_slice_in_dim(rows, me * width, width, 1)]
    for mask in range(1, count):
        part = lax.dynamic_slice_in_dim(rows, (me ^ mask) * width, width, 1)
        pieces.append(swapped(part, "mp", mask))
    return jnp.concatenate(pieces, 0)


def project_out(heads, weight_pieces, residual):
    count = lax.axis_size("mp")
    pieces = [heads] + [swapped(heads, "mp", mask) for mask in range(1, count)]
    terms = jnp.dot(
        jnp.concatenate(pieces, 1), weight_pieces, preferred_element_type=jnp.float32
    )
    return (residual.astype(jnp.float32) + terms).astype(jnp.bfloat16)


def earlier_frames(pair, frames):
    pieces = [pair]
    for step in range(1, WIN // frames + 1):
        pieces.insert(0, passed_along((pair[0], pair[1]), "tm", step))
    key_vals = jnp.concatenate([piece[0] for piece in pieces], 1)
    masks = jnp.concatenate([piece[1] for piece in pieces], 1)
    return (key_vals, masks)


def window_attend(queries, key_vals, masks, wins):
    count_q = queries.shape[1]
    count_k = key_vals.shape[1]
    dist = jnp.arange(count_q)[:, None] + (count_k - count_q) - jnp.arange(count_k)[None, :]

    def one_clip(items):
        query, pairs, kvalid = items
        keys = pairs[:, :, 0]
        values = pairs[:, :, 1]
        allowed = (
            (dist >= 0)
            & (dist < wins[:, :, None, None])
            & ((kvalid[None, None, None, :] == 1) | (dist == 0))
        )
        scores = jnp.einsum(
            "qkgd,ckd->kgqc", query, keys, preferred_element_type=jnp.float32
        ) * HEAD_DIM ** (-0.5)
        top = jnp.max(jnp.where(allowed, scores, -1e30), axis=-1, keepdims=True)
        exps = jnp.where(allowed, jnp.exp(scores - top), 0.0)
        total = jnp.sum(exps, axis=-1)
        weights = exps.astype(jnp.bfloat16)
        summed = jnp.einsum("kgqc,ckd->qkgd", weights, values, preferred_element_type=jnp.float32)
        return (summed / jnp.transpose(total, (2, 0, 1))[..., None]).astype(jnp.bfloat16)

    outputs = lax.map(one_clip, (queries, key_vals, masks))
    return outputs.reshape(outputs.shape[0] * outputs.shape[1], -1)


def body(motion, valid, windows, gains, w_self_in, w_self_out, w_cross_in, w_cross_out):
    clips = motion.shape[1]
    frames = motion.shape[2]
    count = clips * frames
    group = HEADS // KV_HEADS
    local_heads = w_self_out.shape[0] // HEAD_DIM
    local_groups = local_heads // group
    wins = lax.dynamic_slice_in_dim(
        windows, lax.axis_index("mp") * local_heads, local_heads, 0
    ).reshape(local_groups, group)
    own_valid = valid[0]
    residual = motion.reshape(count, motion.shape[3])
    self_out_w = out_weight(w_self_out)
    cross_out_w = out_weight(w_cross_out)
    full = gathered_mp(residual)
    normed = rms_normed(full, gains[0])
    self_proj = project_in(normed, w_self_in).reshape(
        clips, frames, local_groups, group + 2, HEAD_DIM
    )
    self_pair = self_proj[:, :, :, group:]
    key_vals, masks = earlier_frames((self_pair, own_valid), frames)
    self_heads = window_attend(self_proj[:, :, :, :group], key_vals, masks, wins)
    hidden = project_out(self_heads, self_out_w, residual)
    hidden_full = gathered_mp(hidden)
    normed2 = rms_normed(hidden_full, gains[1])
    cross_proj = project_in(normed2, w_cross_in).reshape(
        clips, frames, local_groups, group + 2, HEAD_DIM
    )
    cross_pair = cross_proj[:, :, :, group:]
    partner = swapped((cross_pair, own_valid), "person", 1)
    partner_vals, partner_masks = earlier_frames(partner, frames)
    cross_heads = window_attend(cross_proj[:, :, :, :group], partner_vals, partner_masks, wins)
    mixed = project_out(cross_heads, cross_out_w, hidden)
    return mixed.reshape(motion.shape)


def solution(mesh):
    in_specs = (
        P("person", None, "tm", "mp"),
        P("person", None, "tm"),
        P(),
        P(),
        P("tm", "mp"),
        P("mp", "tm"),
        P("tm", "mp"),
        P("mp", "tm"),
    )
    out_specs = P("person", None, "tm", "mp")
    return jax.shard_map(body, mesh=mesh, in_specs=in_specs, out_specs=out_specs, check_vma=False)
```

```python
import jax
import jax.numpy as jnp
from jax import lax
from jax.sharding import PartitionSpec as P

D = 2048
HEADS = 32
KV_HEADS = 8
HEAD_DIM = 64
WIN = 512


EPS = 1e-05


def passed_along(value, axis, steps):
    count = lax.axis_size(axis)
    leading, last = (max(0, -steps), min(count, count - steps))
    return lax.ppermute(value, axis, [(source, source + steps) for source in range(leading, last)])


def swapped(value, axis, mask):
    pairs = [(source, source ^ mask) for source in range(lax.axis_size(axis))]
    return lax.ppermute(value, axis, pairs)


def gathered_mp(block):
    count = lax.axis_size("mp")
    me = lax.axis_index("mp")
    width = block.shape[-1]
    full = jnp.zeros(block.shape[:-1] + (width * count,), block.dtype)
    zeros = (0,) * (block.ndim - 1)
    full = lax.dynamic_update_slice(full, block, zeros + (me * width,))
    for mask in range(1, count):
        piece = swapped(block, "mp", mask)
        full = lax.dynamic_update_slice(full, piece, zeros + ((me ^ mask) * width,))
    return full


def rms_normed(rows, gain):
    values = rows.astype(jnp.float32)
    scale = lax.rsqrt(jnp.mean(values * values, axis=-1, keepdims=True) + EPS)
    return (values * scale * gain).astype(jnp.bfloat16)


def gathered_weights(weights):
    count = lax.axis_size("tm")
    flat = jnp.concatenate([w.reshape(-1) for w in weights])
    every = lax.all_gather(flat, "tm", axis=0, tiled=False)
    out, start = [], 0
    for w in weights:
        size = w.size
        part = every[:, start:start + size].reshape((count,) + w.shape)
        start += size
        out.append(part)
    return out


def project_in(normed_rows, weight):
    total = jnp.dot(normed_rows, weight, preferred_element_type=jnp.float32)
    return total.astype(jnp.bfloat16)


def out_weight(weight):
    count = lax.axis_size("mp")
    me = lax.axis_index("mp")
    rows = jnp.transpose(weight, (1, 0, 2)).reshape(weight.shape[1], -1)
    width = rows.shape[1] // count
    pieces = [lax.dynamic_slice_in_dim(rows, me * width, width, 1)]
    for mask in range(1, count):
        part = lax.dynamic_slice_in_dim(rows, (me ^ mask) * width, width, 1)
        pieces.append(swapped(part, "mp", mask))
    return jnp.concatenate(pieces, 0)


def project_out(heads, weight_pieces, residual):
    count = lax.axis_size("mp")
    pieces = [heads] + [swapped(heads, "mp", mask) for mask in range(1, count)]
    terms = jnp.dot(
        jnp.concatenate(pieces, 1), weight_pieces, preferred_element_type=jnp.float32
    )
    return (residual.astype(jnp.float32) + terms).astype(jnp.bfloat16)


def earlier_frames(pair, frames):
    pieces = [pair]
    for step in range(1, WIN // frames + 1):
        pieces.insert(0, passed_along((pair[0], pair[1]), "tm", step))
    key_vals = jnp.concatenate([piece[0] for piece in pieces], 1)
    masks = jnp.concatenate([piece[1] for piece in pieces], 1)
    return (key_vals, masks)


def window_attend(queries, key_vals, masks, wins):
    count_q = queries.shape[1]
    count_k = key_vals.shape[1]
    dist = jnp.arange(count_q)[:, None] + (count_k - count_q) - jnp.arange(count_k)[None, :]

    def one_clip(items):
        query, pairs, kvalid = items
        keys = pairs[:, :, 0]
        values = pairs[:, :, 1]
        allowed = (
            (dist >= 0)
            & (dist < wins[:, :, None, None])
            & ((kvalid[None, None, None, :] == 1) | (dist == 0))
        )
        scores = jnp.einsum(
            "qkgd,ckd->kgqc", query, keys, preferred_element_type=jnp.float32
        ) * HEAD_DIM ** (-0.5)
        top = jnp.max(jnp.where(allowed, scores, -1e30), axis=-1, keepdims=True)
        exps = jnp.where(allowed, jnp.exp(scores - top), 0.0)
        total = jnp.sum(exps, axis=-1)
        weights = exps.astype(jnp.bfloat16)
        summed = jnp.einsum("kgqc,ckd->qkgd", weights, values, preferred_element_type=jnp.float32)
        return (summed / jnp.transpose(total, (2, 0, 1))[..., None]).astype(jnp.bfloat16)

    outputs = lax.map(one_clip, (queries, key_vals, masks))
    return outputs.reshape(outputs.shape[0] * outputs.shape[1], -1)


def body(motion, valid, windows, gains, w_self_in, w_self_out, w_cross_in, w_cross_out):
    clips = motion.shape[1]
    frames = motion.shape[2]
    count = clips * frames
    group = HEADS // KV_HEADS
    local_heads = w_self_out.shape[0] // HEAD_DIM
    local_groups = local_heads // group
    wins = lax.dynamic_slice_in_dim(
        windows, lax.axis_index("mp") * local_heads, local_heads, 0
    ).reshape(local_groups, group)
    own_valid = valid[0]
    residual = motion.reshape(count, motion.shape[3])
    self_in_w, self_out_w, cross_in_w, cross_out_w = gathered_weights(
        (w_self_in, w_self_out, w_cross_in, w_cross_out)
    )
    self_in_w = self_in_w.reshape(-1, self_in_w.shape[2])
    cross_in_w = cross_in_w.reshape(-1, cross_in_w.shape[2])
    self_out_w = out_weight(self_out_w)
    cross_out_w = out_weight(cross_out_w)
    full = gathered_mp(residual)
    normed = rms_normed(full, gains[0])
    self_proj = project_in(normed, self_in_w).reshape(
        clips, frames, local_groups, group + 2, HEAD_DIM
    )
    self_pair = self_proj[:, :, :, group:]
    key_vals, masks = earlier_frames((self_pair, own_valid), frames)
    self_heads = window_attend(self_proj[:, :, :, :group], key_vals, masks, wins)
    hidden = project_out(self_heads, self_out_w, residual)
    hidden_full = gathered_mp(hidden)
    normed2 = rms_normed(hidden_full, gains[1])
    cross_proj = project_in(normed2, cross_in_w).reshape(
        clips, frames, local_groups, group + 2, HEAD_DIM
    )
    cross_pair = cross_proj[:, :, :, group:]
    partner = swapped((cross_pair, own_valid), "person", 1)
    partner_vals, partner_masks = earlier_frames(partner, frames)
    cross_heads = window_attend(cross_proj[:, :, :, :group], partner_vals, partner_masks, wins)
    mixed = project_out(cross_heads, cross_out_w, hidden)
    return mixed.reshape(motion.shape)


def solution(mesh):
    in_specs = (
        P("person", None, "tm", "mp"),
        P("person", None, "tm"),
        P(),
        P(),
        P("tm", "mp"),
        P("mp", "tm"),
        P("tm", "mp"),
        P("mp", "tm"),
    )
    out_specs = P("person", None, "tm", "mp")
    return jax.shard_map(body, mesh=mesh, in_specs=in_specs, out_specs=out_specs, check_vma=False)
```

```python
import jax
import jax.numpy as jnp
from jax import lax
from jax.sharding import PartitionSpec as P

D = 2048
HEADS = 32
KV_HEADS = 8
HEAD_DIM = 64
WIN = 512


EPS = 1e-05


def passed_along(value, axis, steps):
    count = lax.axis_size(axis)
    leading, last = (max(0, -steps), min(count, count - steps))
    return lax.ppermute(value, axis, [(source, source + steps) for source in range(leading, last)])


def swapped(value, axis, mask):
    pairs = [(source, source ^ mask) for source in range(lax.axis_size(axis))]
    return lax.ppermute(value, axis, pairs)


def gathered_mp(block):
    count = lax.axis_size("mp")
    me = lax.axis_index("mp")
    width = block.shape[-1]
    full = jnp.zeros(block.shape[:-1] + (width * count,), block.dtype)
    zeros = (0,) * (block.ndim - 1)
    full = lax.dynamic_update_slice(full, block, zeros + (me * width,))
    for mask in range(1, count):
        piece = swapped(block, "mp", mask)
        full = lax.dynamic_update_slice(full, piece, zeros + ((me ^ mask) * width,))
    return full


def rms_normed(rows, gain):
    values = rows.astype(jnp.float32)
    scale = lax.rsqrt(jnp.mean(values * values, axis=-1, keepdims=True) + EPS)
    return (values * scale * gain).astype(jnp.bfloat16)


def project_in(normed_rows, weight):
    total = jnp.dot(normed_rows, weight, preferred_element_type=jnp.float32)
    return total.astype(jnp.bfloat16)


def out_weight(columns):
    count = lax.axis_size("mp")
    me = lax.axis_index("mp")
    width = columns.shape[0] // count
    pieces = [lax.dynamic_slice_in_dim(columns, me * width, width, 0)]
    for mask in range(1, count):
        part = lax.dynamic_slice_in_dim(columns, (me ^ mask) * width, width, 0)
        pieces.append(swapped(part, "mp", mask))
    return jnp.concatenate(pieces, 1)


def project_out(heads, weight_pieces, residual):
    count = lax.axis_size("mp")
    pieces = [heads] + [swapped(heads, "mp", mask) for mask in range(1, count)]
    terms = lax.dot_general(
        jnp.concatenate(pieces, 1), weight_pieces, (((1,), (1,)), ((), ())),
        preferred_element_type=jnp.float32,
    )
    return (residual.astype(jnp.float32) + terms).astype(jnp.bfloat16)


def earlier_frames(pair, frames):
    pieces = [pair]
    for step in range(1, WIN // frames + 1):
        pieces.insert(0, passed_along((pair[0], pair[1]), "tm", step))
    key_vals = jnp.concatenate([piece[0] for piece in pieces], 1)
    masks = jnp.concatenate([piece[1] for piece in pieces], 1)
    return (key_vals, masks)


def window_attend(queries, key_vals, masks, wins):
    count_q = queries.shape[1]
    count_k = key_vals.shape[1]
    dist = jnp.arange(count_q)[:, None] + (count_k - count_q) - jnp.arange(count_k)[None, :]

    def one_clip(items):
        query, pairs, kvalid = items
        keys = pairs[:, :, 0]
        values = pairs[:, :, 1]
        allowed = (
            (dist >= 0)
            & (dist < wins[:, :, None, None])
            & ((kvalid[None, None, None, :] == 1) | (dist == 0))
        )
        scores = jnp.einsum(
            "qkgd,ckd->kgqc", query, keys, preferred_element_type=jnp.float32
        ) * HEAD_DIM ** (-0.5)
        top = jnp.max(jnp.where(allowed, scores, -1e30), axis=-1, keepdims=True)
        exps = jnp.where(allowed, jnp.exp(scores - top), 0.0)
        total = jnp.sum(exps, axis=-1)
        weights = exps.astype(jnp.bfloat16)
        summed = jnp.einsum("kgqc,ckd->qkgd", weights, values, preferred_element_type=jnp.float32)
        return (summed / jnp.transpose(total, (2, 0, 1))[..., None]).astype(jnp.bfloat16)

    outputs = lax.map(one_clip, (queries, key_vals, masks))
    return outputs.reshape(outputs.shape[0] * outputs.shape[1], -1)


def body(motion, valid, windows, gains, w_self_in, w_self_out, w_cross_in, w_cross_out):
    clips = motion.shape[1]
    frames = motion.shape[2]
    group = HEADS // KV_HEADS
    local_heads = w_self_out.shape[0] // HEAD_DIM
    local_groups = local_heads // group
    wins = lax.dynamic_slice_in_dim(
        windows, lax.axis_index("mp") * local_heads, local_heads, 0
    ).reshape(local_groups, group)
    local = jnp.concatenate([w_self_in, w_cross_in, w_self_out.T, w_cross_out.T], 1)
    every = lax.all_gather(local, "tm", axis=0, tiled=True)
    cols_in = w_self_in.shape[1]
    rows_out = w_self_out.shape[0]
    self_in_w = every[:, :cols_in]
    cross_in_w = every[:, cols_in:2 * cols_in]
    self_out_w = out_weight(every[:, 2 * cols_in:2 * cols_in + rows_out])
    cross_out_w = out_weight(every[:, 2 * cols_in + rows_out:])

    outputs = []
    for clip in range(clips):
        own_valid = valid[0, clip][None]
        residual = motion[0, clip]
        full = gathered_mp(residual)
        normed = rms_normed(full, gains[0])
        self_proj = project_in(normed, self_in_w).reshape(
            1, frames, local_groups, group + 2, HEAD_DIM
        )
        self_pair = self_proj[:, :, :, group:]
        key_vals, masks = earlier_frames((self_pair, own_valid), frames)
        self_heads = window_attend(self_proj[:, :, :, :group], key_vals, masks, wins)
        hidden = project_out(self_heads, self_out_w, residual)
        hidden_full = gathered_mp(hidden)
        normed2 = rms_normed(hidden_full, gains[1])
        cross_proj = project_in(normed2, cross_in_w).reshape(
            1, frames, local_groups, group + 2, HEAD_DIM
        )
        cross_pair = cross_proj[:, :, :, group:]
        partner = swapped((cross_pair, own_valid), "person", 1)
        partner_vals, partner_masks = earlier_frames(partner, frames)
        cross_heads = window_attend(cross_proj[:, :, :, :group], partner_vals, partner_masks, wins)
        outputs.append(project_out(cross_heads, cross_out_w, hidden))
    return jnp.stack(outputs, 0)[None]


def solution(mesh):
    in_specs = (
        P("person", None, "tm", "mp"),
        P("person", None, "tm"),
        P(),
        P(),
        P("tm", "mp"),
        P("mp", "tm"),
        P("tm", "mp"),
        P("mp", "tm"),
    )
    out_specs = P("person", None, "tm", "mp")
    return jax.shard_map(body, mesh=mesh, in_specs=in_specs, out_specs=out_specs, check_vma=False)
```

```python
import jax
import jax.numpy as jnp
from jax import lax
from jax.sharding import PartitionSpec as P

D = 2048
HEADS = 32
KV_HEADS = 8
HEAD_DIM = 64
WIN = 512


EPS = 1e-05


def passed_along(value, axis, steps):
    count = lax.axis_size(axis)
    leading, last = (max(0, -steps), min(count, count - steps))
    return lax.ppermute(value, axis, [(source, source + steps) for source in range(leading, last)])


def swapped(value, axis, mask):
    pairs = [(source, source ^ mask) for source in range(lax.axis_size(axis))]
    return lax.ppermute(value, axis, pairs)


def gathered_mp(block):
    count = lax.axis_size("mp")
    tiled = jnp.concatenate([block] * count, block.ndim - 1)
    return lax.all_to_all(tiled, "mp", block.ndim - 1, block.ndim - 1, tiled=True)


def rms_normed(rows, gain):
    values = rows.astype(jnp.float32)
    scale = lax.rsqrt(jnp.mean(values * values, axis=-1, keepdims=True) + EPS)
    return (values * scale * gain).astype(jnp.bfloat16)


def project_in(normed_rows, weight):
    total = jnp.dot(normed_rows, weight, preferred_element_type=jnp.float32)
    return total.astype(jnp.bfloat16)


def out_weight(columns):
    return lax.all_to_all(columns, "mp", 0, 1, tiled=True)


def project_out(heads, weight_rows, residual):
    terms = lax.dot_general(
        gathered_mp(heads), weight_rows, (((1,), (1,)), ((), ())),
        preferred_element_type=jnp.float32,
    )
    return (residual.astype(jnp.float32) + terms).astype(jnp.bfloat16)


def packed(pair, kvalid):
    flag = jnp.broadcast_to(
        kvalid.astype(pair.dtype)[:, :, None, None, None], pair.shape[:3] + (1, pair.shape[4])
    )
    return jnp.concatenate([pair, flag], 3)


def earlier_frames(block, frames):
    pieces = [block]
    for step in range(1, WIN // frames + 1):
        pieces.insert(0, passed_along(block, "tm", step))
    joined = jnp.concatenate(pieces, 1)
    key_vals = joined[:, :, :, :2]
    masks = (joined[:, :, 0, 2, 0] == 1).astype(jnp.int32)
    return (key_vals, masks)


def window_attend(queries, key_vals, masks, wins):
    count_q = queries.shape[1]
    count_k = key_vals.shape[1]
    dist = jnp.arange(count_q)[:, None] + (count_k - count_q) - jnp.arange(count_k)[None, :]

    def one_clip(items):
        query, pairs, kvalid = items
        keys = pairs[:, :, 0]
        values = pairs[:, :, 1]
        allowed = (
            (dist >= 0)
            & (dist < wins[:, :, None, None])
            & ((kvalid[None, None, None, :] == 1) | (dist == 0))
        )
        scores = jnp.einsum(
            "qkgd,ckd->kgqc", query, keys, preferred_element_type=jnp.float32
        ) * HEAD_DIM ** (-0.5)
        top = jnp.max(jnp.where(allowed, scores, -1e30), axis=-1, keepdims=True)
        exps = jnp.where(allowed, jnp.exp(scores - top), 0.0)
        total = jnp.sum(exps, axis=-1)
        weights = exps.astype(jnp.bfloat16)
        summed = jnp.einsum("kgqc,ckd->qkgd", weights, values, preferred_element_type=jnp.float32)
        return (summed / jnp.transpose(total, (2, 0, 1))[..., None]).astype(jnp.bfloat16)

    outputs = lax.map(one_clip, (queries, key_vals, masks))
    return outputs.reshape(outputs.shape[0] * outputs.shape[1], -1)


def body(motion, valid, windows, gains, w_self_in, w_self_out, w_cross_in, w_cross_out):
    clips = motion.shape[1]
    frames = motion.shape[2]
    group = HEADS // KV_HEADS
    local_heads = w_self_out.shape[0] // HEAD_DIM
    local_groups = local_heads // group
    wins = lax.dynamic_slice_in_dim(
        windows, lax.axis_index("mp") * local_heads, local_heads, 0
    ).reshape(local_groups, group)
    local = jnp.concatenate([w_self_in, w_cross_in, w_self_out.T, w_cross_out.T], 1)
    every = lax.all_gather(local, "tm", axis=0, tiled=True)
    cols_in = w_self_in.shape[1]
    rows_out = w_self_out.shape[0]
    self_in_w = every[:, :cols_in]
    cross_in_w = every[:, cols_in:2 * cols_in]
    self_out_w = out_weight(every[:, 2 * cols_in:2 * cols_in + rows_out])
    cross_out_w = out_weight(every[:, 2 * cols_in + rows_out:])

    outputs = []
    for clip in range(clips):
        own_valid = valid[0, clip][None]
        residual = motion[0, clip]
        full = gathered_mp(residual)
        normed = rms_normed(full, gains[0])
        self_proj = project_in(normed, self_in_w).reshape(
            1, frames, local_groups, group + 2, HEAD_DIM
        )
        self_pair = self_proj[:, :, :, group:]
        key_vals, masks = earlier_frames(packed(self_pair, own_valid), frames)
        self_heads = window_attend(self_proj[:, :, :, :group], key_vals, masks, wins)
        hidden = project_out(self_heads, self_out_w, residual)
        hidden_full = gathered_mp(hidden)
        normed2 = rms_normed(hidden_full, gains[1])
        cross_proj = project_in(normed2, cross_in_w).reshape(
            1, frames, local_groups, group + 2, HEAD_DIM
        )
        cross_pair = cross_proj[:, :, :, group:]
        partner = swapped(packed(cross_pair, own_valid), "person", 1)
        partner_vals, partner_masks = earlier_frames(partner, frames)
        cross_heads = window_attend(cross_proj[:, :, :, :group], partner_vals, partner_masks, wins)
        outputs.append(project_out(cross_heads, cross_out_w, hidden))
    return jnp.stack(outputs, 0)[None]


def solution(mesh):
    in_specs = (
        P("person", None, "tm", "mp"),
        P("person", None, "tm"),
        P(),
        P(),
        P("tm", "mp"),
        P("mp", "tm"),
        P("tm", "mp"),
        P("mp", "tm"),
    )
    out_specs = P("person", None, "tm", "mp")
    return jax.shard_map(body, mesh=mesh, in_specs=in_specs, out_specs=out_specs, check_vma=False)
```

```python
import jax
import jax.numpy as jnp
from jax import lax
from jax.sharding import PartitionSpec as P

D = 2048
HEADS = 32
KV_HEADS = 8
HEAD_DIM = 64
WIN = 512


EPS = 1e-05


def passed_along(value, axis, steps):
    count = lax.axis_size(axis)
    leading, last = (max(0, -steps), min(count, count - steps))
    return lax.ppermute(value, axis, [(source, source + steps) for source in range(leading, last)])


def swapped(value, axis, mask):
    pairs = [(source, source ^ mask) for source in range(lax.axis_size(axis))]
    return lax.ppermute(value, axis, pairs)


def gathered_mp(block):
    count = lax.axis_size("mp")
    me = lax.axis_index("mp")
    width = block.shape[-1]
    full = jnp.zeros(block.shape[:-1] + (width * count,), block.dtype)
    zeros = (0,) * (block.ndim - 1)
    full = lax.dynamic_update_slice(full, block, zeros + (me * width,))
    for mask in range(1, count):
        piece = swapped(block, "mp", mask)
        full = lax.dynamic_update_slice(full, piece, zeros + ((me ^ mask) * width,))
    return full


def rms_normed(rows, gain):
    values = rows.astype(jnp.float32)
    scale = lax.rsqrt(jnp.mean(values * values, axis=-1, keepdims=True) + EPS)
    return (values * scale * gain).astype(jnp.bfloat16)


def project_in(normed_rows, weight):
    total = jnp.dot(normed_rows, weight, preferred_element_type=jnp.float32)
    return total.astype(jnp.bfloat16)


def out_weight(columns):
    count = lax.axis_size("mp")
    me = lax.axis_index("mp")
    width = columns.shape[0] // count
    pieces = [lax.dynamic_slice_in_dim(columns, me * width, width, 0)]
    for mask in range(1, count):
        part = lax.dynamic_slice_in_dim(columns, (me ^ mask) * width, width, 0)
        pieces.append(swapped(part, "mp", mask))
    return jnp.concatenate(pieces, 1)


def project_out(heads, weight_pieces, residual):
    count = lax.axis_size("mp")
    pieces = [heads] + [swapped(heads, "mp", mask) for mask in range(1, count)]
    terms = lax.dot_general(
        jnp.concatenate(pieces, 1), weight_pieces, (((1,), (1,)), ((), ())),
        preferred_element_type=jnp.float32,
    )
    return (residual.astype(jnp.float32) + terms).astype(jnp.bfloat16)


def packed(pair, kvalid):
    flag = jnp.broadcast_to(
        kvalid.astype(pair.dtype)[:, :, None, None, None], pair.shape[:3] + (1, pair.shape[4])
    )
    return jnp.concatenate([pair, flag], 3)


def earlier_frames(block, frames, flip):
    slabs = lax.axis_size("tm")
    persons = lax.axis_size("person")
    pieces = []
    for step in range(0, WIN // frames + 1):
        if step == 0 and flip == 0:
            pieces.append(block)
            continue
        pairs = [
            (p * slabs + t, (p ^ flip) * slabs + t + step)
            for p in range(persons)
            for t in range(slabs - step)
        ]
        pieces.append(lax.ppermute(block, ("person", "tm"), pairs))
    joined = jnp.concatenate(pieces[::-1], 1)
    key_vals = joined[:, :, :, :2]
    masks = (joined[:, :, 0, 2, 0] == 1).astype(jnp.int32)
    return (key_vals, masks)


def window_attend(queries, key_vals, masks, wins):
    count_q = queries.shape[1]
    count_k = key_vals.shape[1]
    dist = jnp.arange(count_q)[:, None] + (count_k - count_q) - jnp.arange(count_k)[None, :]

    def one_clip(items):
        query, pairs, kvalid = items
        keys = pairs[:, :, 0]
        values = pairs[:, :, 1]
        allowed = (
            (dist >= 0)
            & (dist < wins[:, :, None, None])
            & ((kvalid[None, None, None, :] == 1) | (dist == 0))
        )
        scores = jnp.einsum(
            "qkgd,ckd->kgqc", query, keys, preferred_element_type=jnp.float32
        ) * HEAD_DIM ** (-0.5)
        top = jnp.max(jnp.where(allowed, scores, -1e30), axis=-1, keepdims=True)
        exps = jnp.where(allowed, jnp.exp(scores - top), 0.0)
        total = jnp.sum(exps, axis=-1)
        weights = exps.astype(jnp.bfloat16)
        summed = jnp.einsum("kgqc,ckd->qkgd", weights, values, preferred_element_type=jnp.float32)
        return (summed / jnp.transpose(total, (2, 0, 1))[..., None]).astype(jnp.bfloat16)

    outputs = lax.map(one_clip, (queries, key_vals, masks))
    return outputs.reshape(outputs.shape[0] * outputs.shape[1], -1)


def body(motion, valid, windows, gains, w_self_in, w_self_out, w_cross_in, w_cross_out):
    clips = motion.shape[1]
    frames = motion.shape[2]
    group = HEADS // KV_HEADS
    local_heads = w_self_out.shape[0] // HEAD_DIM
    local_groups = local_heads // group
    wins = lax.dynamic_slice_in_dim(
        windows, lax.axis_index("mp") * local_heads, local_heads, 0
    ).reshape(local_groups, group)
    local = jnp.concatenate([w_self_in, w_cross_in, w_self_out.T, w_cross_out.T], 1)
    every = lax.all_gather(local, "tm", axis=0, tiled=True)
    cols_in = w_self_in.shape[1]
    rows_out = w_self_out.shape[0]
    self_in_w = every[:, :cols_in]
    cross_in_w = every[:, cols_in:2 * cols_in]
    self_out_w = out_weight(every[:, 2 * cols_in:2 * cols_in + rows_out])
    cross_out_w = out_weight(every[:, 2 * cols_in + rows_out:])

    outputs = []
    for clip in range(clips):
        own_valid = valid[0, clip][None]
        residual = motion[0, clip]
        full = gathered_mp(residual)
        normed = rms_normed(full, gains[0])
        self_proj = project_in(normed, self_in_w).reshape(
            1, frames, local_groups, group + 2, HEAD_DIM
        )
        self_pair = self_proj[:, :, :, group:]
        key_vals, masks = earlier_frames(packed(self_pair, own_valid), frames, 0)
        self_heads = window_attend(self_proj[:, :, :, :group], key_vals, masks, wins)
        hidden = project_out(self_heads, self_out_w, residual)
        hidden_full = gathered_mp(hidden)
        normed2 = rms_normed(hidden_full, gains[1])
        cross_proj = project_in(normed2, cross_in_w).reshape(
            1, frames, local_groups, group + 2, HEAD_DIM
        )
        cross_pair = cross_proj[:, :, :, group:]
        partner_vals, partner_masks = earlier_frames(packed(cross_pair, own_valid), frames, 1)
        cross_heads = window_attend(cross_proj[:, :, :, :group], partner_vals, partner_masks, wins)
        outputs.append(project_out(cross_heads, cross_out_w, hidden))
    return jnp.stack(outputs, 0)[None]


def solution(mesh):
    in_specs = (
        P("person", None, "tm", "mp"),
        P("person", None, "tm"),
        P(),
        P(),
        P("tm", "mp"),
        P("mp", "tm"),
        P("tm", "mp"),
        P("mp", "tm"),
    )
    out_specs = P("person", None, "tm", "mp")
    return jax.shard_map(body, mesh=mesh, in_specs=in_specs, out_specs=out_specs, check_vma=False)
```

```python
import jax
import jax.numpy as jnp
from jax import lax
from jax.sharding import PartitionSpec as P

D = 2048
HEADS = 32
KV_HEADS = 8
HEAD_DIM = 64
WIN = 512


EPS = 1e-05


def passed_along(value, axis, steps):
    count = lax.axis_size(axis)
    leading, last = (max(0, -steps), min(count, count - steps))
    return lax.ppermute(value, axis, [(source, source + steps) for source in range(leading, last)])


def swapped(value, axis, mask):
    pairs = [(source, source ^ mask) for source in range(lax.axis_size(axis))]
    return lax.ppermute(value, axis, pairs)


def gathered_mp(block):
    count = lax.axis_size("mp")
    me = lax.axis_index("mp")
    width = block.shape[-1]
    full = jnp.zeros(block.shape[:-1] + (width * count,), block.dtype)
    zeros = (0,) * (block.ndim - 1)
    full = lax.dynamic_update_slice(full, block, zeros + (me * width,))
    for mask in range(1, count):
        piece = swapped(block, "mp", mask)
        full = lax.dynamic_update_slice(full, piece, zeros + ((me ^ mask) * width,))
    return full


def rms_normed(rows, gain):
    values = rows.astype(jnp.float32)
    scale = lax.rsqrt(jnp.mean(values * values, axis=-1, keepdims=True) + EPS)
    return (values * scale * gain).astype(jnp.bfloat16)


def project_in(normed_rows, weight):
    total = jnp.dot(normed_rows, weight, preferred_element_type=jnp.float32)
    return total.astype(jnp.bfloat16)


def out_weight(columns):
    count = lax.axis_size("mp")
    me = lax.axis_index("mp")
    width = columns.shape[0] // count
    pieces = [lax.dynamic_slice_in_dim(columns, me * width, width, 0)]
    for mask in range(1, count):
        part = lax.dynamic_slice_in_dim(columns, (me ^ mask) * width, width, 0)
        pieces.append(swapped(part, "mp", mask))
    return jnp.concatenate(pieces, 1)


def project_out(heads, weight_pieces, residual):
    count = lax.axis_size("mp")
    pieces = [heads] + [swapped(heads, "mp", mask) for mask in range(1, count)]
    terms = lax.dot_general(
        jnp.concatenate(pieces, 1), weight_pieces, (((1,), (1,)), ((), ())),
        preferred_element_type=jnp.float32,
    )
    return (residual.astype(jnp.float32) + terms).astype(jnp.bfloat16)


def earlier_frames(pair, frames):
    pieces = [pair]
    for step in range(1, WIN // frames + 1):
        pieces.insert(0, passed_along((pair[0], pair[1]), "tm", step))
    key_vals = jnp.concatenate([piece[0] for piece in pieces], 1)
    masks = jnp.concatenate([piece[1] for piece in pieces], 1)
    return (key_vals, masks)


def window_attend(queries, key_vals, masks, wins):
    count_q = queries.shape[1]
    count_k = key_vals.shape[1]
    dist = jnp.arange(count_q)[:, None] + (count_k - count_q) - jnp.arange(count_k)[None, :]

    def one_clip(items):
        query, pairs, kvalid = items
        keys = pairs[:, :, 0]
        values = pairs[:, :, 1]
        allowed = (
            (dist >= 0)
            & (dist < wins[:, :, None, None])
            & ((kvalid[None, None, None, :] == 1) | (dist == 0))
        )
        scores = jnp.einsum(
            "qkgd,ckd->kgqc", query, keys, preferred_element_type=jnp.float32
        ) * HEAD_DIM ** (-0.5)
        top = jnp.max(jnp.where(allowed, scores, -1e30), axis=-1, keepdims=True)
        exps = jnp.where(allowed, jnp.exp(scores - top), 0.0)
        total = jnp.sum(exps, axis=-1)
        weights = exps.astype(jnp.bfloat16)
        summed = jnp.einsum("kgqc,ckd->qkgd", weights, values, preferred_element_type=jnp.float32)
        return (summed / jnp.transpose(total, (2, 0, 1))[..., None]).astype(jnp.bfloat16)

    outputs = lax.map(one_clip, (queries, key_vals, masks))
    return outputs.reshape(outputs.shape[0] * outputs.shape[1], -1)


def body(motion, valid, windows, gains, w_self_in, w_self_out, w_cross_in, w_cross_out):
    clips = motion.shape[1]
    frames = motion.shape[2]
    group = HEADS // KV_HEADS
    local_heads = w_self_out.shape[0] // HEAD_DIM
    local_groups = local_heads // group
    wins = lax.dynamic_slice_in_dim(
        windows, lax.axis_index("mp") * local_heads, local_heads, 0
    ).reshape(local_groups, group)
    cols_in = w_self_in.shape[1]
    self_every = lax.all_gather(
        jnp.concatenate([w_self_in, w_self_out.T], 1), "tm", axis=0, tiled=True
    )
    cross_every = lax.all_gather(
        jnp.concatenate([w_cross_in, w_cross_out.T], 1), "tm", axis=0, tiled=True
    )
    self_in_w = self_every[:, :cols_in]
    cross_in_w = cross_every[:, :cols_in]
    self_out_w = out_weight(self_every[:, cols_in:])
    cross_out_w = out_weight(cross_every[:, cols_in:])

    outputs = []
    for clip in range(clips):
        own_valid = valid[0, clip][None]
        residual = motion[0, clip]
        full = gathered_mp(residual)
        normed = rms_normed(full, gains[0])
        self_proj = project_in(normed, self_in_w).reshape(
            1, frames, local_groups, group + 2, HEAD_DIM
        )
        self_pair = self_proj[:, :, :, group:]
        key_vals, masks = earlier_frames((self_pair, own_valid), frames)
        self_heads = window_attend(self_proj[:, :, :, :group], key_vals, masks, wins)
        hidden = project_out(self_heads, self_out_w, residual)
        hidden_full = gathered_mp(hidden)
        normed2 = rms_normed(hidden_full, gains[1])
        cross_proj = project_in(normed2, cross_in_w).reshape(
            1, frames, local_groups, group + 2, HEAD_DIM
        )
        cross_pair = cross_proj[:, :, :, group:]
        partner = swapped((cross_pair, own_valid), "person", 1)
        partner_vals, partner_masks = earlier_frames(partner, frames)
        cross_heads = window_attend(cross_proj[:, :, :, :group], partner_vals, partner_masks, wins)
        outputs.append(project_out(cross_heads, cross_out_w, hidden))
    return jnp.stack(outputs, 0)[None]


def solution(mesh):
    in_specs = (
        P("person", None, "tm", "mp"),
        P("person", None, "tm"),
        P(),
        P(),
        P("tm", "mp"),
        P("mp", "tm"),
        P("tm", "mp"),
        P("mp", "tm"),
    )
    out_specs = P("person", None, "tm", "mp")
    return jax.shard_map(body, mesh=mesh, in_specs=in_specs, out_specs=out_specs, check_vma=False)
```

```python
import jax
import jax.numpy as jnp
from jax import lax
from jax.sharding import PartitionSpec as P

D = 2048
HEADS = 32
KV_HEADS = 8
HEAD_DIM = 64
WIN = 512


EPS = 1e-05


def passed_along(value, axis, steps):
    count = lax.axis_size(axis)
    leading, last = (max(0, -steps), min(count, count - steps))
    return lax.ppermute(value, axis, [(source, source + steps) for source in range(leading, last)])


def swapped(value, axis, mask):
    pairs = [(source, source ^ mask) for source in range(lax.axis_size(axis))]
    return lax.ppermute(value, axis, pairs)


def gathered_mp(block):
    count = lax.axis_size("mp")
    me = lax.axis_index("mp")
    width = block.shape[-1]
    full = jnp.zeros(block.shape[:-1] + (width * count,), block.dtype)
    zeros = (0,) * (block.ndim - 1)
    full = lax.dynamic_update_slice(full, block, zeros + (me * width,))
    for mask in range(1, count):
        piece = swapped(block, "mp", mask)
        full = lax.dynamic_update_slice(full, piece, zeros + ((me ^ mask) * width,))
    return full


def rms_normed(rows, gain):
    values = rows.astype(jnp.float32)
    scale = lax.rsqrt(jnp.mean(values * values, axis=-1, keepdims=True) + EPS)
    return (values * scale * gain).astype(jnp.bfloat16)


def project_in(normed_rows, weight):
    total = jnp.dot(normed_rows, weight, preferred_element_type=jnp.float32)
    return total.astype(jnp.bfloat16)


def out_weight(columns):
    count = lax.axis_size("mp")
    me = lax.axis_index("mp")
    width = columns.shape[0] // count
    pieces = [lax.dynamic_slice_in_dim(columns, me * width, width, 0)]
    for mask in range(1, count):
        part = lax.dynamic_slice_in_dim(columns, (me ^ mask) * width, width, 0)
        pieces.append(swapped(part, "mp", mask))
    return jnp.concatenate(pieces, 1)


def project_out(heads, weight_pieces, residual):
    count = lax.axis_size("mp")
    pieces = [heads] + [swapped(heads, "mp", mask) for mask in range(1, count)]
    terms = lax.dot_general(
        jnp.concatenate(pieces, 1), weight_pieces, (((1,), (1,)), ((), ())),
        preferred_element_type=jnp.float32,
    )
    return (residual.astype(jnp.float32) + terms).astype(jnp.bfloat16)


def packed(pair, kvalid):
    flag = jnp.broadcast_to(
        kvalid.astype(pair.dtype)[:, :, None, None, None], pair.shape[:3] + (1, pair.shape[4])
    )
    return jnp.concatenate([pair, flag], 3)


def earlier_frames(block, frames):
    pieces = [block]
    for step in range(1, WIN // frames + 1):
        pieces.insert(0, passed_along(block, "tm", step))
    joined = jnp.concatenate(pieces, 1)
    key_vals = joined[:, :, :, :2]
    masks = (joined[:, :, 0, 2, 0] == 1).astype(jnp.int32)
    return (key_vals, masks)


def window_attend(queries, key_vals, masks, wins):
    count_q = queries.shape[1]
    count_k = key_vals.shape[1]
    dist = jnp.arange(count_q)[:, None] + (count_k - count_q) - jnp.arange(count_k)[None, :]

    def one_clip(items):
        query, pairs, kvalid = items
        keys = pairs[:, :, 0]
        values = pairs[:, :, 1]
        allowed = (
            (dist >= 0)
            & (dist < wins[:, :, None, None])
            & ((kvalid[None, None, None, :] == 1) | (dist == 0))
        )
        scores = jnp.einsum(
            "qkgd,ckd->kgqc", query, keys, preferred_element_type=jnp.float32
        ) * HEAD_DIM ** (-0.5)
        top = jnp.max(jnp.where(allowed, scores, -1e30), axis=-1, keepdims=True)
        exps = jnp.where(allowed, jnp.exp(scores - top), 0.0)
        total = jnp.sum(exps, axis=-1)
        weights = exps.astype(jnp.bfloat16)
        summed = jnp.einsum("kgqc,ckd->qkgd", weights, values, preferred_element_type=jnp.float32)
        return (summed / jnp.transpose(total, (2, 0, 1))[..., None]).astype(jnp.bfloat16)

    outputs = lax.map(one_clip, (queries, key_vals, masks))
    return outputs.reshape(outputs.shape[0] * outputs.shape[1], -1)


def body(motion, valid, windows, gains, w_self_in, w_self_out, w_cross_in, w_cross_out):
    clips = motion.shape[1]
    frames = motion.shape[2]
    group = HEADS // KV_HEADS
    local_heads = w_self_out.shape[0] // HEAD_DIM
    local_groups = local_heads // group
    wins = lax.dynamic_slice_in_dim(
        windows, lax.axis_index("mp") * local_heads, local_heads, 0
    ).reshape(local_groups, group)
    cols_in = w_self_in.shape[1]
    self_every = lax.all_gather(
        jnp.concatenate([w_self_in, w_self_out.T], 1), "tm", axis=0, tiled=True
    )
    cross_every = lax.all_gather(
        jnp.concatenate([w_cross_in, w_cross_out.T], 1), "tm", axis=0, tiled=True
    )
    self_in_w = self_every[:, :cols_in]
    cross_in_w = cross_every[:, :cols_in]
    self_out_w = out_weight(self_every[:, cols_in:])
    cross_out_w = out_weight(cross_every[:, cols_in:])

    outputs = []
    for clip in range(clips):
        own_valid = valid[0, clip][None]
        residual = motion[0, clip]
        full = gathered_mp(residual)
        normed = rms_normed(full, gains[0])
        self_proj = project_in(normed, self_in_w).reshape(
            1, frames, local_groups, group + 2, HEAD_DIM
        )
        self_pair = self_proj[:, :, :, group:]
        key_vals, masks = earlier_frames(packed(self_pair, own_valid), frames)
        self_heads = window_attend(self_proj[:, :, :, :group], key_vals, masks, wins)
        hidden = project_out(self_heads, self_out_w, residual)
        hidden_full = gathered_mp(hidden)
        normed2 = rms_normed(hidden_full, gains[1])
        cross_proj = project_in(normed2, cross_in_w).reshape(
            1, frames, local_groups, group + 2, HEAD_DIM
        )
        cross_pair = cross_proj[:, :, :, group:]
        partner = swapped(packed(cross_pair, own_valid), "person", 1)
        partner_vals, partner_masks = earlier_frames(partner, frames)
        cross_heads = window_attend(cross_proj[:, :, :, :group], partner_vals, partner_masks, wins)
        outputs.append(project_out(cross_heads, cross_out_w, hidden))
    return jnp.stack(outputs, 0)[None]


def solution(mesh):
    in_specs = (
        P("person", None, "tm", "mp"),
        P("person", None, "tm"),
        P(),
        P(),
        P("tm", "mp"),
        P("mp", "tm"),
        P("tm", "mp"),
        P("mp", "tm"),
    )
    out_specs = P("person", None, "tm", "mp")
    return jax.shard_map(body, mesh=mesh, in_specs=in_specs, out_specs=out_specs, check_vma=False)
```

```python
import jax
import jax.numpy as jnp
from jax import lax
from jax.sharding import PartitionSpec as P

D = 2048
HEADS = 32
KV_HEADS = 8
HEAD_DIM = 64
WIN = 512


EPS = 1e-05


def passed_along(value, axis, steps):
    count = lax.axis_size(axis)
    leading, last = (max(0, -steps), min(count, count - steps))
    return lax.ppermute(value, axis, [(source, source + steps) for source in range(leading, last)])


def swapped(value, axis, mask):
    pairs = [(source, source ^ mask) for source in range(lax.axis_size(axis))]
    return lax.ppermute(value, axis, pairs)


def gathered_mp(block):
    count = lax.axis_size("mp")
    me = lax.axis_index("mp")
    width = block.shape[-1]
    full = jnp.zeros(block.shape[:-1] + (width * count,), block.dtype)
    zeros = (0,) * (block.ndim - 1)
    full = lax.dynamic_update_slice(full, block, zeros + (me * width,))
    for mask in range(1, count):
        piece = swapped(block, "mp", mask)
        full = lax.dynamic_update_slice(full, piece, zeros + ((me ^ mask) * width,))
    return full


def rms_normed(rows, gain):
    values = rows.astype(jnp.float32)
    scale = lax.rsqrt(jnp.mean(values * values, axis=-1, keepdims=True) + EPS)
    return (values * scale * gain).astype(jnp.bfloat16)


def project_in(normed_rows, weight):
    total = jnp.dot(normed_rows, weight, preferred_element_type=jnp.float32)
    return total.astype(jnp.bfloat16)


def out_weight(columns):
    count = lax.axis_size("mp")
    me = lax.axis_index("mp")
    width = columns.shape[0] // count
    pieces = [lax.dynamic_slice_in_dim(columns, me * width, width, 0)]
    for mask in range(1, count):
        part = lax.dynamic_slice_in_dim(columns, (me ^ mask) * width, width, 0)
        pieces.append(swapped(part, "mp", mask))
    return jnp.concatenate(pieces, 1)


def project_out(heads, weight_pieces, residual):
    count = lax.axis_size("mp")
    pieces = [heads] + [swapped(heads, "mp", mask) for mask in range(1, count)]
    terms = lax.dot_general(
        jnp.concatenate(pieces, 1), weight_pieces, (((1,), (1,)), ((), ())),
        preferred_element_type=jnp.float32,
    )
    return (residual.astype(jnp.float32) + terms).astype(jnp.bfloat16)


def earlier_frames(pair, frames):
    pieces = [pair]
    for step in range(1, WIN // frames + 1):
        pieces.insert(0, passed_along((pair[0], pair[1]), "tm", step))
    key_vals = jnp.concatenate([piece[0] for piece in pieces], 1)
    masks = jnp.concatenate([piece[1] for piece in pieces], 1)
    return (key_vals, masks)


def window_attend(queries, key_vals, masks, wins):
    count_q = queries.shape[1]
    count_k = key_vals.shape[1]
    dist = jnp.arange(count_q)[:, None] + (count_k - count_q) - jnp.arange(count_k)[None, :]

    def one_clip(items):
        query, pairs, kvalid = items
        keys = pairs[:, :, 0]
        values = pairs[:, :, 1]
        allowed = (
            (dist >= 0)
            & (dist < wins[:, :, None, None])
            & ((kvalid[None, None, None, :] == 1) | (dist == 0))
        )
        scores = jnp.einsum(
            "qkgd,ckd->kgqc", query, keys, preferred_element_type=jnp.float32
        ) * HEAD_DIM ** (-0.5)
        top = jnp.max(jnp.where(allowed, scores, -1e30), axis=-1, keepdims=True)
        exps = jnp.where(allowed, jnp.exp(scores - top), 0.0)
        total = jnp.sum(exps, axis=-1)
        weights = exps.astype(jnp.bfloat16)
        summed = jnp.einsum("kgqc,ckd->qkgd", weights, values, preferred_element_type=jnp.float32)
        return (summed / jnp.transpose(total, (2, 0, 1))[..., None]).astype(jnp.bfloat16)

    outputs = lax.map(one_clip, (queries, key_vals, masks))
    return outputs.reshape(outputs.shape[0] * outputs.shape[1], -1)


def halves_attend(queries, key_vals, masks, wins):
    count_q = queries.shape[1]
    part = count_q // 2
    span = key_vals.shape[1] - count_q + part
    outs = []
    for h in range(2):
        outs.append(window_attend(
            queries[:, h * part:(h + 1) * part],
            key_vals[:, h * part:h * part + span],
            masks[:, h * part:h * part + span],
            wins,
        ))
    return jnp.concatenate(outs, 0)


def body(motion, valid, windows, gains, w_self_in, w_self_out, w_cross_in, w_cross_out):
    clips = motion.shape[1]
    frames = motion.shape[2]
    group = HEADS // KV_HEADS
    local_heads = w_self_out.shape[0] // HEAD_DIM
    local_groups = local_heads // group
    wins = lax.dynamic_slice_in_dim(
        windows, lax.axis_index("mp") * local_heads, local_heads, 0
    ).reshape(local_groups, group)
    cols_in = w_self_in.shape[1]
    self_every = lax.all_gather(
        jnp.concatenate([w_self_in, w_self_out.T], 1), "tm", axis=0, tiled=True
    )
    cross_every = lax.all_gather(
        jnp.concatenate([w_cross_in, w_cross_out.T], 1), "tm", axis=0, tiled=True
    )
    self_in_w = self_every[:, :cols_in]
    cross_in_w = cross_every[:, :cols_in]
    self_out_w = out_weight(self_every[:, cols_in:])
    cross_out_w = out_weight(cross_every[:, cols_in:])

    outputs = []
    for clip in range(clips):
        own_valid = valid[0, clip][None]
        residual = motion[0, clip]
        full = gathered_mp(residual)
        normed = rms_normed(full, gains[0])
        self_proj = project_in(normed, self_in_w).reshape(
            1, frames, local_groups, group + 2, HEAD_DIM
        )
        self_pair = self_proj[:, :, :, group:]
        key_vals, masks = earlier_frames((self_pair, own_valid), frames)
        self_heads = halves_attend(self_proj[:, :, :, :group], key_vals, masks, wins)
        hidden = project_out(self_heads, self_out_w, residual)
        hidden_full = gathered_mp(hidden)
        normed2 = rms_normed(hidden_full, gains[1])
        cross_proj = project_in(normed2, cross_in_w).reshape(
            1, frames, local_groups, group + 2, HEAD_DIM
        )
        cross_pair = cross_proj[:, :, :, group:]
        partner = swapped((cross_pair, own_valid), "person", 1)
        partner_vals, partner_masks = earlier_frames(partner, frames)
        cross_heads = halves_attend(cross_proj[:, :, :, :group], partner_vals, partner_masks, wins)
        outputs.append(project_out(cross_heads, cross_out_w, hidden))
    return jnp.stack(outputs, 0)[None]


def solution(mesh):
    in_specs = (
        P("person", None, "tm", "mp"),
        P("person", None, "tm"),
        P(),
        P(),
        P("tm", "mp"),
        P("mp", "tm"),
        P("tm", "mp"),
        P("mp", "tm"),
    )
    out_specs = P("person", None, "tm", "mp")
    return jax.shard_map(body, mesh=mesh, in_specs=in_specs, out_specs=out_specs, check_vma=False)
```

```python
import jax
import jax.numpy as jnp
from jax import lax
from jax.sharding import PartitionSpec as P

D = 2048
HEADS = 32
KV_HEADS = 8
HEAD_DIM = 64
WIN = 512


EPS = 1e-05


def passed_along(value, axis, steps):
    count = lax.axis_size(axis)
    leading, last = (max(0, -steps), min(count, count - steps))
    return lax.ppermute(value, axis, [(source, source + steps) for source in range(leading, last)])


def swapped(value, axis, mask):
    pairs = [(source, source ^ mask) for source in range(lax.axis_size(axis))]
    return lax.ppermute(value, axis, pairs)


def gathered_mp(block):
    count = lax.axis_size("mp")
    me = lax.axis_index("mp")
    width = block.shape[-1]
    full = jnp.zeros(block.shape[:-1] + (width * count,), block.dtype)
    zeros = (0,) * (block.ndim - 1)
    full = lax.dynamic_update_slice(full, block, zeros + (me * width,))
    for mask in range(1, count):
        piece = swapped(block, "mp", mask)
        full = lax.dynamic_update_slice(full, piece, zeros + ((me ^ mask) * width,))
    return full


def rms_normed(rows, gain):
    values = rows.astype(jnp.float32)
    scale = lax.rsqrt(jnp.mean(values * values, axis=-1, keepdims=True) + EPS)
    return (values * scale * gain).astype(jnp.bfloat16)


def project_in(normed_rows, weight):
    total = jnp.dot(normed_rows, weight, preferred_element_type=jnp.float32)
    return total.astype(jnp.bfloat16)


def out_weight(columns):
    count = lax.axis_size("mp")
    me = lax.axis_index("mp")
    width = columns.shape[0] // count
    pieces = [lax.dynamic_slice_in_dim(columns, me * width, width, 0)]
    for mask in range(1, count):
        part = lax.dynamic_slice_in_dim(columns, (me ^ mask) * width, width, 0)
        pieces.append(swapped(part, "mp", mask))
    return jnp.concatenate(pieces, 1)


def project_out(heads, weight_pieces, residual):
    count = lax.axis_size("mp")
    pieces = [heads] + [swapped(heads, "mp", mask) for mask in range(1, count)]
    terms = lax.dot_general(
        jnp.concatenate(pieces, 1), weight_pieces, (((1,), (1,)), ((), ())),
        preferred_element_type=jnp.float32,
    )
    return (residual.astype(jnp.float32) + terms).astype(jnp.bfloat16)


def earlier_frames(pair, frames):
    pieces = [pair]
    for step in range(1, WIN // frames + 1):
        pieces.insert(0, passed_along((pair[0], pair[1]), "tm", step))
    key_vals = jnp.concatenate([piece[0] for piece in pieces], 1)
    masks = jnp.concatenate([piece[1] for piece in pieces], 1)
    return (key_vals, masks)


def window_attend(queries, key_vals, masks, wins):
    count_q = queries.shape[1]
    count_k = key_vals.shape[1]
    dist = jnp.arange(count_q)[:, None] + (count_k - count_q) - jnp.arange(count_k)[None, :]

    def one_clip(items):
        query, pairs, kvalid = items
        keys = pairs[:, :, 0]
        values = pairs[:, :, 1]
        allowed = (
            (dist >= 0)
            & (dist < wins[:, :, None, None])
            & ((kvalid[None, None, None, :] == 1) | (dist == 0))
        )
        scores = jnp.einsum(
            "qkgd,ckd->kgqc", query, keys, preferred_element_type=jnp.float32
        ) * HEAD_DIM ** (-0.5)
        top = jnp.max(jnp.where(allowed, scores, -1e30), axis=-1, keepdims=True)
        exps = jnp.where(allowed, jnp.exp(scores - top), 0.0)
        total = jnp.sum(exps, axis=-1)
        weights = exps.astype(jnp.bfloat16)
        summed = jnp.einsum("kgqc,ckd->qkgd", weights, values, preferred_element_type=jnp.float32)
        return (summed / jnp.transpose(total, (2, 0, 1))[..., None]).astype(jnp.bfloat16)

    outputs = lax.map(one_clip, (queries, key_vals, masks))
    return outputs.reshape(outputs.shape[0] * outputs.shape[1], -1)


def body(motion, valid, windows, gains, w_self_in, w_self_out, w_cross_in, w_cross_out):
    clips = motion.shape[1]
    frames = motion.shape[2]
    group = HEADS // KV_HEADS
    local_heads = w_self_out.shape[0] // HEAD_DIM
    local_groups = local_heads // group
    wins = lax.dynamic_slice_in_dim(
        windows, lax.axis_index("mp") * local_heads, local_heads, 0
    ).reshape(local_groups, group)
    cols_in = w_self_in.shape[1]
    self_every = lax.all_gather(
        jnp.concatenate([w_self_in, w_self_out.T], 1), "tm", axis=0, tiled=True
    )
    cross_every = lax.all_gather(
        jnp.concatenate([w_cross_in, w_cross_out.T], 1), "tm", axis=0, tiled=True
    )
    self_in_w = self_every[:, :cols_in]
    cross_in_w = cross_every[:, :cols_in]
    self_out_w = out_weight(self_every[:, cols_in:])
    cross_out_w = out_weight(cross_every[:, cols_in:])

    projs = []
    for clip in range(clips):
        full = gathered_mp(motion[0, clip])
        normed = rms_normed(full, gains[0])
        projs.append(project_in(normed, self_in_w).reshape(
            1, frames, local_groups, group + 2, HEAD_DIM
        ))
    all_vals, all_masks = earlier_frames(
        (jnp.concatenate([p[:, :, :, group:] for p in projs], 0), valid[0]), frames
    )
    outputs = []
    for clip in range(clips):
        own_valid = valid[0, clip][None]
        residual = motion[0, clip]
        self_proj = projs[clip]
        key_vals = all_vals[clip:clip + 1]
        masks = all_masks[clip:clip + 1]
        self_heads = window_attend(self_proj[:, :, :, :group], key_vals, masks, wins)
        hidden = project_out(self_heads, self_out_w, residual)
        hidden_full = gathered_mp(hidden)
        normed2 = rms_normed(hidden_full, gains[1])
        cross_proj = project_in(normed2, cross_in_w).reshape(
            1, frames, local_groups, group + 2, HEAD_DIM
        )
        cross_pair = cross_proj[:, :, :, group:]
        partner = swapped((cross_pair, own_valid), "person", 1)
        partner_vals, partner_masks = earlier_frames(partner, frames)
        cross_heads = window_attend(cross_proj[:, :, :, :group], partner_vals, partner_masks, wins)
        outputs.append(project_out(cross_heads, cross_out_w, hidden))
    return jnp.stack(outputs, 0)[None]


def solution(mesh):
    in_specs = (
        P("person", None, "tm", "mp"),
        P("person", None, "tm"),
        P(),
        P(),
        P("tm", "mp"),
        P("mp", "tm"),
        P("tm", "mp"),
        P("mp", "tm"),
    )
    out_specs = P("person", None, "tm", "mp")
    return jax.shard_map(body, mesh=mesh, in_specs=in_specs, out_specs=out_specs, check_vma=False)
```
